256 devices in a mesh: seq: 32 (over y, z), grp: 8 (over x, core).
Axes of the slice: x: 4, y: 4, z: 8, core: 2. Of those that a mesh axis runs over, the one named last changes fastest.
Arguments:
- query: bfloat16 [8, 4096, 2048], P('grp', 'seq'), may hold values from -6 to 6
- key_in: bfloat16 [8, 4096, 2048], P('grp', 'seq'), may hold values from -6 to 6
- value: bfloat16 [8, 4096, 2048], P('grp', 'seq'), may hold values from -6 to 6
- cotangent: bfloat16 [8, 4096, 2048], P('grp', 'seq'), may hold values from -6 to 6
- routes: int32 [8, 4096, 6], P('grp', 'seq'), may hold values from 0 to 63, as said below
- gates: float32 [8, 4096, 6], P('grp', 'seq'), may hold values from 0.01 to 0.1
- hidden: bfloat16 [8, 4096, 6, 704], P('grp', 'seq'), may hold values from -6 to 6
Outputs:
- attention_out: bfloat16 [8, 4096, 2048], P('grp', 'seq')
- grad_query: bfloat16 [8, 4096, 2048], P('grp', 'seq')
- grad_key: bfloat16 [8, 4096, 2048], P('grp', 'seq')
- grad_value: bfloat16 [8, 4096, 2048], P('grp', 'seq')
- expert_grad: bfloat16 [64, 704, 2048], P('seq', 'grp')
The draws below stay inside these ranges and needn't reach their ends.
Inputs may be any that keep to these rules, and one draw needn't show every extreme that they name: `routes`: the 6 experts of a token differ. Among the 128 tokens of one device (aligned blocks of the positions of a sequence) no expert is named more than 32 times, and in every sequence some expert is named exactly 32 times by the tokens of each device. Expert ids are small integers and may be packed several to a word whenever they are sent.
All inputs are finite; a program needn't handle non-finite values.
Results may differ from the reference program's by a relative error of at most 0.04.
Values may be sent and summed in bfloat16 or wider, within the bound.
No kernel may reach another device: no remote copies, remote signals or barrier semaphores. Data moves between devices by JAX's collectives and lax.ppermute only.
A program may use at most 192 MiB of HBM per device.

```python
import math
import jax
import jax.numpy as jnp
from jax import lax

HEADS = 16
DH = 128
F = 704
TOPK = 6
TOK_DEV = 128
DW = 2048
EXPERTS = 64
SEQS = 8
LENGTH = 4096
CAP = 32
N_SEQ = 32


def draw_routes(key, part):
    per_seq = LENGTH // TOK_DEV
    blocks = SEQS * per_seq
    slots = TOK_DEV * TOPK
    seq_keys = jax.random.split(jax.random.fold_in(key, 11), SEQS)
    hot_seq = jax.vmap(lambda single: jax.random.randint(single, (), 0, EXPERTS))(seq_keys)
    block_keys = jax.random.split(jax.random.fold_in(key, 17), blocks)
    hot_block = jnp.repeat(hot_seq, per_seq)

    def one_block(block_key, hottest):
        keys = jax.random.split(block_key, 5)
        order = jax.random.permutation(keys[0], EXPERTS)
        table = order[jnp.arange(slots) % EXPERTS].reshape(TOK_DEV, TOPK)
        has_hot = jnp.any(table == hottest, axis=1)
        base_hot = jnp.sum((table == hottest).astype(jnp.int32))
        free_rows = jnp.logical_not(has_hot)
        ranking = jnp.cumsum(free_rows.astype(jnp.int32))
        chosen = free_rows & (ranking <= CAP - base_hot)
        table = table.at[:, 0].set(jnp.where(chosen, hottest, table[:, 0]))
        second = (hottest + 1 + jax.random.randint(keys[1], (), 0, EXPERTS - 1)) % EXPERTS
        has_second = jnp.any(table == second, axis=1)
        now_hot = jnp.any(table == hottest, axis=1)
        base_second = jnp.sum((table == second).astype(jnp.int32))
        extra = jax.random.randint(keys[2], (), 0, CAP - base_second + 1)
        free_two = jnp.logical_not(has_second) & jnp.logical_not(now_hot)
        ranking_two = jnp.cumsum(free_two.astype(jnp.int32))
        chosen_two = free_two & (ranking_two <= extra)
        table = table.at[:, 1].set(jnp.where(chosen_two, second, table[:, 1]))
        shuffle = jax.random.permutation(keys[3], TOK_DEV)
        table = table[shuffle]
        rolls = jax.random.randint(keys[4], (TOK_DEV,), 0, TOPK)
        columns = (jnp.arange(TOPK)[None, :] + rolls[:, None]) % TOPK
        return jnp.take_along_axis(table, columns, axis=1)
    result = jax.vmap(one_block)(block_keys, hot_block)
    return result.reshape(SEQS, LENGTH, TOPK).astype(jnp.int32)


def block_levels(rng, extent, cuts, smallest, high):
    loudness = 1.0
    for dim, shards_of in cuts:
        draws = jax.random.uniform(jax.random.fold_in(jax.random.fold_in(rng, 6), dim), (shards_of,), jnp.float32, smallest / len(cuts), high / len(cuts))
        loudness = loudness * jnp.repeat(jnp.exp(draws), extent[dim] // shards_of).reshape((-1,) + (1,) * (len(extent) - 1 - dim))
    return loudness


def normal_values(own_key, dims, scale, bound, pieces=(), kind=jnp.bfloat16):
    values = jax.random.normal(own_key, dims, jnp.float32) * scale
    if len(pieces) > 0:
        values = block_levels(own_key, dims, pieces, -0.22, 0.18) * values
    return jnp.clip(values, min=-bound, max=bound).astype(kind)


def setup_inputs(seed: int = 0) -> dict:
    key_list = jax.random.split(jax.random.key(seed), 8)
    return {
        "query": normal_values(key_list[0], (SEQS, LENGTH, DW), 1.0, 6.0, ((0, 8), (1, 32))),
        "key_in": normal_values(key_list[1], (SEQS, LENGTH, DW), 1.0, 6.0, ((0, 8), (1, 32))),
        "value": normal_values(key_list[2], (SEQS, LENGTH, DW), 1.0, 6.0, ((0, 8), (1, 32))),
        "cotangent": normal_values(key_list[3], (SEQS, LENGTH, DW), 1.0, 6.0, ((0, 8), (1, 32))),
        "routes": draw_routes(jax.random.fold_in(key_list[7], 71), 0),
        "gates": jnp.clip(jnp.exp(math.log(0.1) - 2.3025851 * jax.random.uniform(key_list[5], (SEQS, LENGTH, TOPK), jnp.float32) ** block_levels(key_list[5], (SEQS, LENGTH, TOPK), ((0, 8), (1, 32)), -0.2, 0.2)), 0.01, 0.1),
        "hidden": normal_values(key_list[6], (SEQS, LENGTH, TOPK, F), 1.0, 6.0, ((0, 8), (1, 32))),
    }


PRECISE = lax.Precision.HIGHEST

def attention_pass(query, key_in, value, cotangent):
    blocks = LENGTH // TOK_DEV

    def split_heads(array):
        return array.astype(jnp.float32).reshape(SEQS, blocks, TOK_DEV, HEADS, DH).transpose(1, 0, 2, 3, 4)
    query_full = split_heads(query)
    key_full = split_heads(key_in)
    value_full = split_heads(value)
    grad_out = split_heads(cotangent)
    position = jnp.arange(LENGTH, dtype=jnp.int32).reshape(blocks, TOK_DEV)
    scaling = 1.0 / jnp.sqrt(DH * (position + 1).astype(jnp.float32))
    causal = jnp.tril(jnp.ones((TOK_DEV, TOK_DEV), jnp.float32))

    def forward_step(prefix_state, inputs):
        query_blk, key_blk, value_blk, grad_blk, scale_blk = inputs
        row_scale = scale_blk[None, :, None, None]
        scores = jnp.einsum('sthd,suhd->shtu', query_blk, key_blk, precision=PRECISE) * causal
        outputs = jnp.einsum('shtu,suhe->sthe', scores, value_blk, precision=PRECISE)
        outputs = (outputs + jnp.einsum('sthd,shde->sthe', query_blk, prefix_state, precision=PRECISE)) * row_scale
        grad_scores = jnp.einsum('sthe,suhe->shtu', grad_blk, value_blk, precision=PRECISE) * causal
        grad_q = jnp.einsum('shtu,suhd->sthd', grad_scores, key_blk, precision=PRECISE)
        grad_q = (grad_q + jnp.einsum('sthe,shde->sthd', grad_blk, prefix_state, precision=PRECISE)) * row_scale
        new_state = prefix_state + jnp.einsum('suhd,suhe->shde', key_blk, value_blk, precision=PRECISE)
        return (new_state, (outputs, grad_q))

    def backward_step(after_state, inputs):
        query_blk, key_blk, value_blk, grad_blk, scale_blk = inputs
        col_scale = scale_blk[None, None, :, None]
        weighted = jnp.einsum('sthd,suhd->shtu', query_blk, key_blk, precision=PRECISE) * causal * col_scale
        grad_weighted = jnp.einsum('sthe,suhe->shtu', grad_blk, value_blk, precision=PRECISE) * causal * col_scale
        grad_k = jnp.einsum('shtu,sthd->suhd', grad_weighted, query_blk, precision=PRECISE)
        grad_k = grad_k + jnp.einsum('suhe,shde->suhd', value_blk, after_state, precision=PRECISE)
        grad_v = jnp.einsum('shtu,sthe->suhe', weighted, grad_blk, precision=PRECISE)
        grad_v = grad_v + jnp.einsum('suhd,shde->suhe', key_blk, after_state, precision=PRECISE)
        scaled_query = query_blk * scale_blk[None, :, None, None]
        new_state = after_state + jnp.einsum('sthd,sthe->shde', scaled_query, grad_blk, precision=PRECISE)
        return (new_state, (grad_k, grad_v))
    empty = jnp.zeros((SEQS, HEADS, DH, DH), jnp.float32)
    inputs = (query_full, key_full, value_full, grad_out, scaling)
    final_fwd, (outputs, grad_q) = lax.scan(forward_step, empty, inputs)
    final_bwd, (grad_k, grad_v) = lax.scan(backward_step, empty, inputs, reverse=True)

    def join_heads(array):
        return array.transpose(1, 0, 2, 3, 4).reshape(SEQS, LENGTH, HEADS * DH).astype(jnp.bfloat16)
    return (join_heads(outputs), join_heads(grad_q), join_heads(grad_k), join_heads(grad_v))

def group_gradient(route_seq, gate_seq, hidden_seq, cot_seq):
    count = LENGTH * TOPK
    span = N_SEQ * CAP
    flat_ids = route_seq.reshape(count).astype(jnp.int32)
    scaled = (gate_seq.reshape(count, 1) * hidden_seq.reshape(count, F).astype(jnp.float32)).astype(jnp.bfloat16)
    order = jnp.argsort(flat_ids, stable=True).astype(jnp.int32)
    sorted_ids = flat_ids[order]
    expert_ids = jnp.arange(EXPERTS, dtype=jnp.int32)
    starts = jnp.searchsorted(sorted_ids, expert_ids, side='left').astype(jnp.int32)
    ends = jnp.searchsorted(sorted_ids, expert_ids, side='right').astype(jnp.int32)
    sorted_rows = jnp.concatenate([scaled[order], jnp.zeros((span, F), jnp.bfloat16)], axis=0)
    sorted_tokens = jnp.concatenate([order // TOPK, jnp.zeros((span,), jnp.int32)], axis=0).astype(jnp.int32)

    def one_expert(expert):
        start = starts[expert]
        rows_h = lax.dynamic_slice_in_dim(sorted_rows, start, span, 0)
        rows_t = lax.dynamic_slice_in_dim(sorted_tokens, start, span, 0)
        live = jnp.arange(span, dtype=jnp.int32) < ends[expert] - start
        rows_h = jnp.where(live[:, None], rows_h.astype(jnp.float32), 0.0)
        rows_d = jnp.take(cot_seq, rows_t, axis=0).astype(jnp.float32)
        return jnp.dot(rows_h.T, rows_d, preferred_element_type=jnp.float32)
    return lax.map(one_expert, expert_ids)

def reference(query, key_in, value, cotangent, routes, gates, hidden):
    attention_out, grad_query, grad_key, grad_value = attention_pass(query, key_in, value, cotangent)

    def accumulate(total, inputs):
        partial_sum = group_gradient(*inputs)
        rounded = lax.optimization_barrier(partial_sum.astype(jnp.bfloat16)).astype(jnp.float32)
        return (total + rounded, jnp.zeros((), jnp.float32))
    start_total = jnp.zeros((EXPERTS, F, HEADS * DH), jnp.float32)
    summed, unused = lax.scan(accumulate, start_total, (routes, gates, hidden, cotangent))
    expert_grad = summed.astype(jnp.bfloat16)
    return (attention_out, grad_query, grad_key, grad_value, expert_grad)
```

```python
import jax
import jax.numpy as jnp
from jax import lax
from jax.sharding import PartitionSpec as P

HEADS = 16
TOPK = 6
EXP_DEV = 2
CAP = 32


PRECISE = lax.Precision.HIGHEST


def exclusive_scan(local_sum, axis, backward):
    count = lax.axis_size(axis)
    window = local_sum
    total = jnp.zeros_like(local_sum)
    shift = 1
    while shift < count:
        if backward:
            pairs = [(src, src - shift) for src in range(shift, count)]
        else:
            pairs = [(src, src + shift) for src in range(count - shift)]
        arrived = lax.ppermute(window.astype(jnp.bfloat16), axis, pairs)
        total = total + arrived.astype(jnp.float32)
        window = local_sum + total
        shift *= 2
    return total


def per_device(query, key_in, value, cotangent, routes, gates, hidden):
    tokens = query.shape[1]
    width = query.shape[2]
    head_dim = width // HEADS
    hidden_units = hidden.shape[3]
    seq_count = lax.axis_size("seq")
    seq_index = lax.axis_index("seq")

    experts_total = EXP_DEV * seq_count
    assigned = tokens * TOPK
    slots = experts_total * CAP
    flat_ids = routes[0].reshape(assigned)
    expert_range = jnp.arange(experts_total, dtype=jnp.int32)
    matches = (flat_ids[:, None] == expert_range[None, :]).astype(jnp.int32)
    ranking = jnp.sum((jnp.cumsum(matches, axis=0) - matches) * matches, axis=1)
    slot_index = flat_ids * CAP + ranking
    slot_range = jnp.arange(slots, dtype=jnp.int32)
    pick = slot_index[None, :] == slot_range[:, None]
    scaled = (
        gates[0].reshape(assigned, 1)
        * hidden[0].reshape(assigned, hidden_units).astype(jnp.float32)
    ).astype(jnp.bfloat16)
    hidden_slots = jnp.dot(
        pick.astype(jnp.bfloat16), scaled, preferred_element_type=jnp.float32
    ).astype(jnp.bfloat16)
    pick_token = jnp.any(pick.reshape(slots, tokens, TOPK), axis=2)
    cot_slots = jnp.dot(
        pick_token.astype(jnp.bfloat16), cotangent[0], preferred_element_type=jnp.float32
    ).astype(jnp.bfloat16)
    hidden_slots = hidden_slots.reshape(seq_count, EXP_DEV, CAP, hidden_units)
    cot_slots = cot_slots.reshape(seq_count, EXP_DEV, CAP, width)
    arrived_hidden = lax.all_to_all(hidden_slots, "seq", split_axis=0, concat_axis=0, tiled=True)
    arrived_cot = lax.all_to_all(cot_slots, "seq", split_axis=0, concat_axis=0, tiled=True)

    query_raw = query[0].reshape(tokens, HEADS, head_dim)
    key_raw = key_in[0].reshape(tokens, HEADS, head_dim)
    value_raw = value[0].reshape(tokens, HEADS, head_dim)
    grad_raw = cotangent[0].reshape(tokens, HEADS, head_dim)
    query_full = query_raw.astype(jnp.float32)
    key_full = key_raw.astype(jnp.float32)
    value_full = value_raw.astype(jnp.float32)
    grad_out = grad_raw.astype(jnp.float32)
    position = seq_index * tokens + jnp.arange(tokens, dtype=jnp.int32)
    scaling = 1.0 / jnp.sqrt(head_dim * (position + 1).astype(jnp.float32))
    row_scale = scaling[:, None, None]
    causal = jnp.tril(jnp.ones((tokens, tokens), jnp.float32))
    state_sum = jnp.einsum("thd,the->hde", key_raw, value_raw, preferred_element_type=jnp.float32)
    grad_sum = jnp.einsum("thd,the->hde", query_full * row_scale, grad_out, precision=PRECISE)
    prefix_state = exclusive_scan(state_sum, "seq", False)
    after_state = exclusive_scan(grad_sum, "seq", True)
    scores = (
        jnp.einsum("thd,uhd->htu", query_raw, key_raw, preferred_element_type=jnp.float32) * causal
    )
    outputs = jnp.einsum("htu,uhe->the", scores, value_full, precision=PRECISE)
    outputs = (
        outputs + jnp.einsum("thd,hde->the", query_full, prefix_state, precision=PRECISE)
    ) * row_scale
    grad_scores = (
        jnp.einsum("the,uhe->htu", grad_raw, value_raw, preferred_element_type=jnp.float32) * causal
    )
    grad_q = jnp.einsum("htu,uhd->thd", grad_scores, key_full, precision=PRECISE)
    grad_q = (
        grad_q + jnp.einsum("the,hde->thd", grad_out, prefix_state, precision=PRECISE)
    ) * row_scale
    col_scale = scaling[None, :, None]
    weighted = scores * col_scale
    grad_weighted = grad_scores * col_scale
    grad_k = jnp.einsum("htu,thd->uhd", grad_weighted, query_full, precision=PRECISE)
    grad_k = grad_k + jnp.einsum("uhe,hde->uhd", value_full, after_state, precision=PRECISE)
    grad_v = jnp.einsum("htu,the->uhe", weighted, grad_out, precision=PRECISE)
    grad_v = grad_v + jnp.einsum("uhd,hde->uhe", key_full, after_state, precision=PRECISE)

    def to_shard(array):
        return array.reshape(1, tokens, width).astype(jnp.bfloat16)

    group_term = jnp.einsum(
        "sxcf,sxcd->xfd", arrived_hidden, arrived_cot, preferred_element_type=jnp.float32
    )
    rounded = lax.optimization_barrier(group_term.astype(jnp.bfloat16)).astype(jnp.float32)
    expert_grad = lax.psum_scatter(
        rounded.astype(jnp.bfloat16), "grp", scatter_dimension=1, tiled=True
    )
    return (to_shard(outputs), to_shard(grad_q), to_shard(grad_k), to_shard(grad_v), expert_grad)


def solution(mesh):
    in_specs = (
        P("grp", "seq", None),
        P("grp", "seq", None),
        P("grp", "seq", None),
        P("grp", "seq", None),
        P("grp", "seq", None),
        P("grp", "seq", None),
        P("grp", "seq", None, None),
    )
    out_specs = (
        P("grp", "seq", None),
        P("grp", "seq", None),
        P("grp", "seq", None),
        P("grp", "seq", None),
        P("seq", "grp", None),
    )
    return jax.shard_map(
        per_device, mesh=mesh, in_specs=in_specs, out_specs=out_specs, check_vma=False
    )
```

```python
import jax
import jax.numpy as jnp
from jax import lax
from jax.sharding import PartitionSpec as P

HEADS = 16
TOPK = 6
EXP_DEV = 2
CAP = 32


PRECISE = lax.Precision.HIGHEST


def exclusive_scan(local_sum, axis, backward):
    count = lax.axis_size(axis)
    window = local_sum
    total = jnp.zeros_like(local_sum)
    shift = 1
    while shift < count:
        if backward:
            pairs = [(src, src - shift) for src in range(shift, count)]
        else:
            pairs = [(src, src + shift) for src in range(count - shift)]
        arrived = lax.ppermute(window.astype(jnp.bfloat16), axis, pairs)
        total = total + arrived.astype(jnp.float32)
        window = local_sum + total
        shift *= 2
    return total


def per_device(query, key_in, value, cotangent, routes, gates, hidden):
    tokens = query.shape[1]
    width = query.shape[2]
    head_dim = width // HEADS
    hidden_units = hidden.shape[3]
    seq_count = lax.axis_size("seq")
    seq_index = lax.axis_index("seq")

    experts_total = EXP_DEV * seq_count
    assigned = tokens * TOPK
    slots = experts_total * CAP
    flat_ids = routes[0].reshape(assigned)
    expert_range = jnp.arange(experts_total, dtype=jnp.int32)
    matches = (flat_ids[:, None] == expert_range[None, :]).astype(jnp.int32)
    ranking = jnp.sum((jnp.cumsum(matches, axis=0) - matches) * matches, axis=1)
    slot_index = flat_ids * CAP + ranking
    slot_range = jnp.arange(slots, dtype=jnp.int32)
    pick = slot_index[None, :] == slot_range[:, None]
    scaled = (
        gates[0].reshape(assigned, 1)
        * hidden[0].reshape(assigned, hidden_units).astype(jnp.float32)
    ).astype(jnp.bfloat16)
    lanes = -(-(hidden_units + 1) // 128) * 128
    token_tag = (jnp.arange(assigned, dtype=jnp.int32) // TOPK + 1).astype(jnp.bfloat16)
    tagged = jnp.concatenate(
        [
            scaled,
            token_tag[:, None],
            jnp.zeros((assigned, lanes - hidden_units - 1), jnp.bfloat16),
        ],
        axis=1,
    )
    hidden_slots = jnp.dot(
        pick.astype(jnp.bfloat16), tagged, preferred_element_type=jnp.float32
    ).astype(jnp.bfloat16)
    hidden_slots = hidden_slots.reshape(seq_count, EXP_DEV, CAP, lanes)
    arrived = lax.all_to_all(hidden_slots, "seq", split_axis=0, concat_axis=0, tiled=True)
    all_cotangent = lax.all_gather(cotangent, "seq", axis=1, tiled=True)[0]
    arrived_hidden = arrived[..., :hidden_units]
    slot_token = jnp.maximum(arrived[..., hidden_units].astype(jnp.int32) - 1, 0)
    wanted = (
        jnp.arange(seq_count, dtype=jnp.int32)[:, None, None] * tokens + slot_token
    ).reshape(-1)
    arrived_cot = jnp.take(all_cotangent, wanted, axis=0).reshape(
        seq_count, EXP_DEV, CAP, width
    )

    query_raw = query[0].reshape(tokens, HEADS, head_dim)
    key_raw = key_in[0].reshape(tokens, HEADS, head_dim)
    value_raw = value[0].reshape(tokens, HEADS, head_dim)
    grad_raw = cotangent[0].reshape(tokens, HEADS, head_dim)
    query_full = query_raw.astype(jnp.float32)
    key_full = key_raw.astype(jnp.float32)
    value_full = value_raw.astype(jnp.float32)
    grad_out = grad_raw.astype(jnp.float32)
    position = seq_index * tokens + jnp.arange(tokens, dtype=jnp.int32)
    scaling = 1.0 / jnp.sqrt(head_dim * (position + 1).astype(jnp.float32))
    row_scale = scaling[:, None, None]
    causal = jnp.tril(jnp.ones((tokens, tokens), jnp.float32))
    state_sum = jnp.einsum("thd,the->hde", key_raw, value_raw, preferred_element_type=jnp.float32)
    grad_sum = jnp.einsum("thd,the->hde", query_full * row_scale, grad_out, precision=PRECISE)
    prefix_state = exclusive_scan(state_sum, "seq", False)
    after_state = exclusive_scan(grad_sum, "seq", True)
    scores = (
        jnp.einsum("thd,uhd->htu", query_raw, key_raw, preferred_element_type=jnp.float32) * causal
    )
    outputs = jnp.einsum("htu,uhe->the", scores, value_full, precision=PRECISE)
    outputs = (
        outputs + jnp.einsum("thd,hde->the", query_full, prefix_state, precision=PRECISE)
    ) * row_scale
    grad_scores = (
        jnp.einsum("the,uhe->htu", grad_raw, value_raw, preferred_element_type=jnp.float32) * causal
    )
    grad_q = jnp.einsum("htu,uhd->thd", grad_scores, key_full, precision=PRECISE)
    grad_q = (
        grad_q + jnp.einsum("the,hde->thd", grad_out, prefix_state, precision=PRECISE)
    ) * row_scale
    col_scale = scaling[None, :, None]
    weighted = scores * col_scale
    grad_weighted = grad_scores * col_scale
    grad_k = jnp.einsum("htu,thd->uhd", grad_weighted, query_full, precision=PRECISE)
    grad_k = grad_k + jnp.einsum("uhe,hde->uhd", value_full, after_state, precision=PRECISE)
    grad_v = jnp.einsum("htu,the->uhe", weighted, grad_out, precision=PRECISE)
    grad_v = grad_v + jnp.einsum("uhd,hde->uhe", key_full, after_state, precision=PRECISE)

    def to_shard(array):
        return array.reshape(1, tokens, width).astype(jnp.bfloat16)

    group_term = jnp.einsum(
        "sxcf,sxcd->xfd", arrived_hidden, arrived_cot, preferred_element_type=jnp.float32
    )
    rounded = lax.optimization_barrier(group_term.astype(jnp.bfloat16)).astype(jnp.float32)
    expert_grad = lax.psum_scatter(
        rounded.astype(jnp.bfloat16), "grp", scatter_dimension=1, tiled=True
    )
    return (to_shard(outputs), to_shard(grad_q), to_shard(grad_k), to_shard(grad_v), expert_grad)


def solution(mesh):
    in_specs = (
        P("grp", "seq", None),
        P("grp", "seq", None),
        P("grp", "seq", None),
        P("grp", "seq", None),
        P("grp", "seq", None),
        P("grp", "seq", None),
        P("grp", "seq", None, None),
    )
    out_specs = (
        P("grp", "seq", None),
        P("grp", "seq", None),
        P("grp", "seq", None),
        P("grp", "seq", None),
        P("seq", "grp", None),
    )
    return jax.shard_map(
        per_device, mesh=mesh, in_specs=in_specs, out_specs=out_specs, check_vma=False
    )
```

```python
import jax
import jax.numpy as jnp
from jax import lax
from jax.sharding import PartitionSpec as P

HEADS = 16
TOPK = 6
EXP_DEV = 2
CAP = 32


PRECISE = lax.Precision.HIGHEST


def exclusive_scan(local_sum, axis, backward, radix=4):
    count = lax.axis_size(axis)
    window = local_sum
    total = jnp.zeros_like(local_sum)
    stride = 1
    while stride < count:
        sent = window.astype(jnp.bfloat16)
        for step in range(1, radix):
            shift = step * stride
            if shift >= count:
                break
            if backward:
                pairs = [(src, src - shift) for src in range(shift, count)]
            else:
                pairs = [(src, src + shift) for src in range(count - shift)]
            total = total + lax.ppermute(sent, axis, pairs).astype(jnp.float32)
        window = local_sum + total
        stride *= radix
    return total


def per_device(query, key_in, value, cotangent, routes, gates, hidden):
    tokens = query.shape[1]
    width = query.shape[2]
    head_dim = width // HEADS
    hidden_units = hidden.shape[3]
    seq_count = lax.axis_size("seq")
    seq_index = lax.axis_index("seq")

    experts_total = EXP_DEV * seq_count
    assigned = tokens * TOPK
    slots = experts_total * CAP
    flat_ids = routes[0].reshape(assigned)
    expert_range = jnp.arange(experts_total, dtype=jnp.int32)
    matches = (flat_ids[:, None] == expert_range[None, :]).astype(jnp.int32)
    ranking = jnp.sum((jnp.cumsum(matches, axis=0) - matches) * matches, axis=1)
    slot_index = flat_ids * CAP + ranking
    slot_range = jnp.arange(slots, dtype=jnp.int32)
    pick = slot_index[None, :] == slot_range[:, None]
    scaled = (
        gates[0].reshape(assigned, 1)
        * hidden[0].reshape(assigned, hidden_units).astype(jnp.float32)
    ).astype(jnp.bfloat16)
    lanes = -(-(hidden_units + 1) // 128) * 128
    token_tag = (jnp.arange(assigned, dtype=jnp.int32) // TOPK + 1).astype(jnp.bfloat16)
    tagged = jnp.concatenate(
        [
            scaled,
            token_tag[:, None],
            jnp.zeros((assigned, lanes - hidden_units - 1), jnp.bfloat16),
        ],
        axis=1,
    )
    hidden_slots = jnp.dot(
        pick.astype(jnp.bfloat16), tagged, preferred_element_type=jnp.float32
    ).astype(jnp.bfloat16)
    hidden_slots = hidden_slots.reshape(seq_count, EXP_DEV, CAP, lanes)
    arrived = lax.all_to_all(hidden_slots, "seq", split_axis=0, concat_axis=0, tiled=True)
    all_cotangent = lax.all_gather(cotangent, "seq", axis=1, tiled=True)[0]
    arrived_hidden = arrived[..., :hidden_units]
    slot_token = jnp.maximum(arrived[..., hidden_units].astype(jnp.int32) - 1, 0)
    wanted = (
        jnp.arange(seq_count, dtype=jnp.int32)[:, None, None] * tokens + slot_token
    ).reshape(-1)

    query_raw = query[0].reshape(tokens, HEADS, head_dim)
    key_raw = key_in[0].reshape(tokens, HEADS, head_dim)
    value_raw = value[0].reshape(tokens, HEADS, head_dim)
    grad_raw = cotangent[0].reshape(tokens, HEADS, head_dim)
    query_full = query_raw.astype(jnp.float32)
    key_full = key_raw.astype(jnp.float32)
    value_full = value_raw.astype(jnp.float32)
    grad_out = grad_raw.astype(jnp.float32)
    position = seq_index * tokens + jnp.arange(tokens, dtype=jnp.int32)
    scaling = 1.0 / jnp.sqrt(head_dim * (position + 1).astype(jnp.float32))
    row_scale = scaling[:, None, None]
    causal = jnp.tril(jnp.ones((tokens, tokens), jnp.float32))
    state_sum = jnp.einsum("thd,the->hde", key_raw, value_raw, preferred_element_type=jnp.float32)
    grad_sum = jnp.einsum("thd,the->hde", query_full * row_scale, grad_out, precision=PRECISE)
    prefix_state = exclusive_scan(state_sum, "seq", False)
    after_state = exclusive_scan(grad_sum, "seq", True)
    scores = (
        jnp.einsum("thd,uhd->htu", query_raw, key_raw, preferred_element_type=jnp.float32) * causal
    )
    outputs = jnp.einsum("htu,uhe->the", scores, value_full, precision=PRECISE)
    outputs = (
        outputs + jnp.einsum("thd,hde->the", query_full, prefix_state, precision=PRECISE)
    ) * row_scale
    grad_scores = (
        jnp.einsum("the,uhe->htu", grad_raw, value_raw, preferred_element_type=jnp.float32) * causal
    )
    grad_q = jnp.einsum("htu,uhd->thd", grad_scores, key_full, precision=PRECISE)
    grad_q = (
        grad_q + jnp.einsum("the,hde->thd", grad_out, prefix_state, precision=PRECISE)
    ) * row_scale
    col_scale = scaling[None, :, None]
    weighted = scores * col_scale
    grad_weighted = grad_scores * col_scale
    grad_k = jnp.einsum("htu,thd->uhd", grad_weighted, query_full, precision=PRECISE)
    grad_k = grad_k + jnp.einsum("uhe,hde->uhd", value_full, after_state, precision=PRECISE)
    grad_v = jnp.einsum("htu,the->uhe", weighted, grad_out, precision=PRECISE)
    grad_v = grad_v + jnp.einsum("uhd,hde->uhe", key_full, after_state, precision=PRECISE)

    def to_shard(array):
        return array.reshape(1, tokens, width).astype(jnp.bfloat16)

    outputs, grad_q, grad_k, grad_v, arrived_hidden, wanted = lax.optimization_barrier(
        (outputs, grad_q, grad_k, grad_v, arrived_hidden, wanted)
    )
    arrived_cot = jnp.take(all_cotangent, wanted, axis=0).reshape(
        seq_count, EXP_DEV, CAP, width
    )
    group_term = jnp.einsum(
        "sxcf,sxcd->xfd", arrived_hidden, arrived_cot, preferred_element_type=jnp.float32
    )
    rounded = lax.optimization_barrier(group_term.astype(jnp.bfloat16)).astype(jnp.float32)
    expert_grad = lax.psum_scatter(
        rounded.astype(jnp.bfloat16), "grp", scatter_dimension=1, tiled=True
    )
    return (to_shard(outputs), to_shard(grad_q), to_shard(grad_k), to_shard(grad_v), expert_grad)


def solution(mesh):
    in_specs = (
        P("grp", "seq", None),
        P("grp", "seq", None),
        P("grp", "seq", None),
        P("grp", "seq", None),
        P("grp", "seq", None),
        P("grp", "seq", None),
        P("grp", "seq", None, None),
    )
    out_specs = (
        P("grp", "seq", None),
        P("grp", "seq", None),
        P("grp", "seq", None),
        P("grp", "seq", None),
        P("seq", "grp", None),
    )
    return jax.shard_map(
        per_device, mesh=mesh, in_specs=in_specs, out_specs=out_specs, check_vma=False
    )
```

```python
import jax
import jax.numpy as jnp
from jax import lax
from jax.sharding import PartitionSpec as P

HEADS = 16
TOPK = 6
EXP_DEV = 2
CAP = 32


PRECISE = lax.Precision.HIGHEST


def per_device(query, key_in, value, cotangent, routes, gates, hidden):
    tokens = query.shape[1]
    width = query.shape[2]
    head_dim = width // HEADS
    hidden_units = hidden.shape[3]
    seq_count = lax.axis_size("seq")
    seq_index = lax.axis_index("seq")

    experts_total = EXP_DEV * seq_count
    assigned = tokens * TOPK
    slots = experts_total * CAP
    flat_ids = routes[0].reshape(assigned)
    expert_range = jnp.arange(experts_total, dtype=jnp.int32)
    matches = (flat_ids[:, None] == expert_range[None, :]).astype(jnp.int32)
    ranking = jnp.sum((jnp.cumsum(matches, axis=0) - matches) * matches, axis=1)
    slot_index = flat_ids * CAP + ranking
    slot_range = jnp.arange(slots, dtype=jnp.int32)
    pick = slot_index[None, :] == slot_range[:, None]
    scaled = (
        gates[0].reshape(assigned, 1)
        * hidden[0].reshape(assigned, hidden_units).astype(jnp.float32)
    ).astype(jnp.bfloat16)
    lanes = -(-(hidden_units + 1) // 128) * 128
    token_tag = (jnp.arange(assigned, dtype=jnp.int32) // TOPK + 1).astype(jnp.bfloat16)
    tagged = jnp.concatenate(
        [
            scaled,
            token_tag[:, None],
            jnp.zeros((assigned, lanes - hidden_units - 1), jnp.bfloat16),
        ],
        axis=1,
    )
    hidden_slots = jnp.dot(
        pick.astype(jnp.bfloat16), tagged, preferred_element_type=jnp.float32
    ).astype(jnp.bfloat16)
    hidden_slots = hidden_slots.reshape(seq_count, EXP_DEV, CAP, lanes)
    arrived = lax.all_to_all(hidden_slots, "seq", split_axis=0, concat_axis=0, tiled=True)
    all_cotangent = lax.all_gather(cotangent, "seq", axis=1, tiled=True)[0]
    arrived_hidden = arrived[..., :hidden_units]
    slot_token = jnp.maximum(arrived[..., hidden_units].astype(jnp.int32) - 1, 0)
    wanted = jnp.arange(seq_count, dtype=jnp.int32)[:, None, None] * tokens + slot_token

    query_raw = query[0].reshape(tokens, HEADS, head_dim)
    key_raw = key_in[0].reshape(tokens, HEADS, head_dim)
    value_raw = value[0].reshape(tokens, HEADS, head_dim)
    grad_raw = cotangent[0].reshape(tokens, HEADS, head_dim)
    query_full = query_raw.astype(jnp.float32)
    key_full = key_raw.astype(jnp.float32)
    value_full = value_raw.astype(jnp.float32)
    grad_out = grad_raw.astype(jnp.float32)
    position = seq_index * tokens + jnp.arange(tokens, dtype=jnp.int32)
    scaling = 1.0 / jnp.sqrt(head_dim * (position + 1).astype(jnp.float32))
    row_scale = scaling[:, None, None]
    causal = jnp.tril(jnp.ones((tokens, tokens), jnp.float32))
    state_sum = jnp.einsum("thd,the->hde", key_raw, value_raw, preferred_element_type=jnp.float32)
    grad_sum = jnp.einsum("thd,the->hde", query_full * row_scale, grad_out, precision=PRECISE)
    state_sum, grad_sum, all_cotangent = lax.optimization_barrier(
        (state_sum, grad_sum, all_cotangent)
    )
    chunks = 4
    chunk = seq_count // chunks
    group_term = jnp.zeros((EXP_DEV, hidden_units, width), jnp.float32)
    prefix_state = jnp.zeros_like(state_sum)
    after_state = jnp.zeros_like(grad_sum)
    fwd_window = state_sum
    bwd_window = grad_sum
    shift = 1
    done_chunks = 0
    while shift < seq_count or done_chunks < chunks:
        fwd_sent = fwd_window.astype(jnp.bfloat16)
        bwd_sent = bwd_window.astype(jnp.bfloat16)
        if done_chunks < chunks:
            low = done_chunks * chunk
            part_hidden, part_wanted, fwd_sent, bwd_sent = lax.optimization_barrier(
                (arrived_hidden[low:low + chunk], wanted[low:low + chunk], fwd_sent, bwd_sent)
            )
        if shift < seq_count:
            fwd_pairs = [(src, src + shift) for src in range(seq_count - shift)]
            bwd_pairs = [(src, src - shift) for src in range(shift, seq_count)]
            fwd_arrived = lax.ppermute(fwd_sent, "seq", fwd_pairs)
            bwd_arrived = lax.ppermute(bwd_sent, "seq", bwd_pairs)
        if done_chunks < chunks:
            rows = jnp.take(all_cotangent, part_wanted.reshape(-1), axis=0).reshape(
                chunk, EXP_DEV, CAP, width
            )
            group_term = group_term + jnp.einsum(
                "sxcf,sxcd->xfd", part_hidden, rows, preferred_element_type=jnp.float32
            )
            done_chunks += 1
        if shift < seq_count:
            prefix_state = prefix_state + fwd_arrived.astype(jnp.float32)
            after_state = after_state + bwd_arrived.astype(jnp.float32)
            fwd_window = state_sum + prefix_state
            bwd_window = grad_sum + after_state
            shift *= 2
    scores = (
        jnp.einsum("thd,uhd->htu", query_raw, key_raw, preferred_element_type=jnp.float32) * causal
    )
    outputs = jnp.einsum("htu,uhe->the", scores, value_full, precision=PRECISE)
    outputs = (
        outputs + jnp.einsum("thd,hde->the", query_full, prefix_state, precision=PRECISE)
    ) * row_scale
    grad_scores = (
        jnp.einsum("the,uhe->htu", grad_raw, value_raw, preferred_element_type=jnp.float32) * causal
    )
    grad_q = jnp.einsum("htu,uhd->thd", grad_scores, key_full, precision=PRECISE)
    grad_q = (
        grad_q + jnp.einsum("the,hde->thd", grad_out, prefix_state, precision=PRECISE)
    ) * row_scale
    col_scale = scaling[None, :, None]
    weighted = scores * col_scale
    grad_weighted = grad_scores * col_scale
    grad_k = jnp.einsum("htu,thd->uhd", grad_weighted, query_full, precision=PRECISE)
    grad_k = grad_k + jnp.einsum("uhe,hde->uhd", value_full, after_state, precision=PRECISE)
    grad_v = jnp.einsum("htu,the->uhe", weighted, grad_out, precision=PRECISE)
    grad_v = grad_v + jnp.einsum("uhd,hde->uhe", key_full, after_state, precision=PRECISE)

    def to_shard(array):
        return array.reshape(1, tokens, width).astype(jnp.bfloat16)

    rounded = lax.optimization_barrier(group_term.astype(jnp.bfloat16)).astype(jnp.float32)
    expert_grad = lax.psum_scatter(
        rounded.astype(jnp.bfloat16), "grp", scatter_dimension=1, tiled=True
    )
    return (to_shard(outputs), to_shard(grad_q), to_shard(grad_k), to_shard(grad_v), expert_grad)


def solution(mesh):
    in_specs = (
        P("grp", "seq", None),
        P("grp", "seq", None),
        P("grp", "seq", None),
        P("grp", "seq", None),
        P("grp", "seq", None),
        P("grp", "seq", None),
        P("grp", "seq", None, None),
    )
    out_specs = (
        P("grp", "seq", None),
        P("grp", "seq", None),
        P("grp", "seq", None),
        P("grp", "seq", None),
        P("seq", "grp", None),
    )
    return jax.shard_map(
        per_device, mesh=mesh, in_specs=in_specs, out_specs=out_specs, check_vma=False
    )
```

```python
import jax
import jax.numpy as jnp
from jax import lax
from jax.sharding import PartitionSpec as P

HEADS = 16
TOPK = 6
EXP_DEV = 2
CAP = 32


PRECISE = lax.Precision.HIGHEST


def per_device(query, key_in, value, cotangent, routes, gates, hidden):
    tokens = query.shape[1]
    width = query.shape[2]
    head_dim = width // HEADS
    hidden_units = hidden.shape[3]
    seq_count = lax.axis_size("seq")
    seq_index = lax.axis_index("seq")

    experts_total = EXP_DEV * seq_count
    assigned = tokens * TOPK
    slots = experts_total * CAP
    flat_ids = routes[0].reshape(assigned)
    expert_range = jnp.arange(experts_total, dtype=jnp.int32)
    matches = (flat_ids[:, None] == expert_range[None, :]).astype(jnp.int32)
    ranking = jnp.sum((jnp.cumsum(matches, axis=0) - matches) * matches, axis=1)
    slot_index = flat_ids * CAP + ranking
    slot_range = jnp.arange(slots, dtype=jnp.int32)
    pick = slot_index[None, :] == slot_range[:, None]
    scaled = (
        gates[0].reshape(assigned, 1)
        * hidden[0].reshape(assigned, hidden_units).astype(jnp.float32)
    ).astype(jnp.bfloat16)
    lanes = -(-(hidden_units + 1) // 128) * 128
    token_tag = (jnp.arange(assigned, dtype=jnp.int32) // TOPK + 1).astype(jnp.bfloat16)
    tagged = jnp.concatenate(
        [
            scaled,
            token_tag[:, None],
            jnp.zeros((assigned, lanes - hidden_units - 1), jnp.bfloat16),
        ],
        axis=1,
    )
    hidden_slots = jnp.dot(
        pick.astype(jnp.bfloat16), tagged, preferred_element_type=jnp.float32
    ).astype(jnp.bfloat16)
    hidden_slots = hidden_slots.reshape(seq_count, EXP_DEV, CAP, lanes)
    arrived = lax.all_to_all(hidden_slots, "seq", split_axis=0, concat_axis=0, tiled=True)
    all_cotangent = lax.all_gather(cotangent, "seq", axis=1, tiled=True)[0]
    arrived_hidden = arrived[..., :hidden_units]
    slot_token = jnp.maximum(arrived[..., hidden_units].astype(jnp.int32) - 1, 0)
    wanted = jnp.arange(seq_count, dtype=jnp.int32)[:, None, None] * tokens + slot_token

    query_raw = query[0].reshape(tokens, HEADS, head_dim)
    key_raw = key_in[0].reshape(tokens, HEADS, head_dim)
    value_raw = value[0].reshape(tokens, HEADS, head_dim)
    grad_raw = cotangent[0].reshape(tokens, HEADS, head_dim)
    query_full = query_raw.astype(jnp.float32)
    key_full = key_raw.astype(jnp.float32)
    value_full = value_raw.astype(jnp.float32)
    grad_out = grad_raw.astype(jnp.float32)
    position = seq_index * tokens + jnp.arange(tokens, dtype=jnp.int32)
    scaling = 1.0 / jnp.sqrt(head_dim * (position + 1).astype(jnp.float32))
    row_scale = scaling[:, None, None]
    causal = jnp.tril(jnp.ones((tokens, tokens), jnp.float32))
    state_sum = jnp.einsum("thd,the->hde", key_raw, value_raw, preferred_element_type=jnp.float32)
    grad_sum = jnp.einsum("thd,the->hde", query_full * row_scale, grad_out, precision=PRECISE)
    scores = (
        jnp.einsum("thd,uhd->htu", query_raw, key_raw, preferred_element_type=jnp.float32) * causal
    )
    grad_scores = (
        jnp.einsum("the,uhe->htu", grad_raw, value_raw, preferred_element_type=jnp.float32) * causal
    )
    col_scale = scaling[None, :, None]
    out_local = jnp.einsum("htu,uhe->the", scores, value_full, precision=PRECISE)
    grad_q_local = jnp.einsum("htu,uhd->thd", grad_scores, key_full, precision=PRECISE)
    grad_k_local = jnp.einsum("htu,thd->uhd", grad_scores * col_scale, query_full, precision=PRECISE)
    grad_v_local = jnp.einsum("htu,the->uhe", scores * col_scale, grad_out, precision=PRECISE)
    (
        state_sum, grad_sum, out_local, grad_q_local, grad_k_local, grad_v_local, all_cotangent
    ) = lax.optimization_barrier(
        (state_sum, grad_sum, out_local, grad_q_local, grad_k_local, grad_v_local, all_cotangent)
    )
    group_term = None
    prefix_state = jnp.zeros_like(state_sum)
    after_state = jnp.zeros_like(grad_sum)
    fwd_window = state_sum
    bwd_window = grad_sum
    shift = 1
    while shift < seq_count:
        fwd_sent = fwd_window.astype(jnp.bfloat16)
        bwd_sent = bwd_window.astype(jnp.bfloat16)
        if group_term is None and shift > 1:
            part_hidden, part_wanted, fwd_sent, bwd_sent = lax.optimization_barrier(
                (arrived_hidden, wanted, fwd_sent, bwd_sent)
            )
        fwd_pairs = [(src, src + shift) for src in range(seq_count - shift)]
        bwd_pairs = [(src, src - shift) for src in range(shift, seq_count)]
        fwd_arrived = lax.ppermute(fwd_sent, "seq", fwd_pairs)
        bwd_arrived = lax.ppermute(bwd_sent, "seq", bwd_pairs)
        if group_term is None and shift > 1:
            rows = jnp.take(all_cotangent, part_wanted.reshape(-1), axis=0).reshape(
                seq_count, EXP_DEV, CAP, width
            )
            group_term = jnp.einsum(
                "sxcf,sxcd->fxd", part_hidden, rows, preferred_element_type=jnp.float32
            )
        prefix_state = prefix_state + fwd_arrived.astype(jnp.float32)
        after_state = after_state + bwd_arrived.astype(jnp.float32)
        fwd_window = state_sum + prefix_state
        bwd_window = grad_sum + after_state
        shift *= 2
    outputs = (
        out_local + jnp.einsum("thd,hde->the", query_full, prefix_state, precision=PRECISE)
    ) * row_scale
    grad_q = (
        grad_q_local + jnp.einsum("the,hde->thd", grad_out, prefix_state, precision=PRECISE)
    ) * row_scale
    grad_k = grad_k_local + jnp.einsum("uhe,hde->uhd", value_full, after_state, precision=PRECISE)
    grad_v = grad_v_local + jnp.einsum("uhd,hde->uhe", key_full, after_state, precision=PRECISE)

    def to_shard(array):
        return array.reshape(1, tokens, width).astype(jnp.bfloat16)

    rounded = lax.optimization_barrier(group_term.astype(jnp.bfloat16)).astype(jnp.float32)
    expert_grad = lax.psum_scatter(
        rounded.astype(jnp.bfloat16), "grp", scatter_dimension=0, tiled=True
    ).transpose(1, 0, 2)
    return (to_shard(outputs), to_shard(grad_q), to_shard(grad_k), to_shard(grad_v), expert_grad)


def solution(mesh):
    in_specs = (
        P("grp", "seq", None),
        P("grp", "seq", None),
        P("grp", "seq", None),
        P("grp", "seq", None),
        P("grp", "seq", None),
        P("grp", "seq", None),
        P("grp", "seq", None, None),
    )
    out_specs = (
        P("grp", "seq", None),
        P("grp", "seq", None),
        P("grp", "seq", None),
        P("grp", "seq", None),
        P("seq", "grp", None),
    )
    return jax.shard_map(
        per_device, mesh=mesh, in_specs=in_specs, out_specs=out_specs, check_vma=False
    )
```

```python
import jax
import jax.numpy as jnp
from jax import lax
from jax.sharding import PartitionSpec as P

HEADS = 16
TOPK = 6
EXP_DEV = 2
CAP = 32


PRECISE = lax.Precision.HIGHEST


def per_device(query, key_in, value, cotangent, routes, gates, hidden):
    tokens = query.shape[1]
    width = query.shape[2]
    head_dim = width // HEADS
    hidden_units = hidden.shape[3]
    seq_count = lax.axis_size("seq")
    seq_index = lax.axis_index("seq")

    experts_total = EXP_DEV * seq_count
    assigned = tokens * TOPK
    slots = experts_total * CAP
    flat_ids = routes[0].reshape(assigned)
    expert_range = jnp.arange(experts_total, dtype=jnp.int32)
    matches = (flat_ids[:, None] == expert_range[None, :]).astype(jnp.int32)
    ranking = jnp.sum((jnp.cumsum(matches, axis=0) - matches) * matches, axis=1)
    slot_index = flat_ids * CAP + ranking
    slot_range = jnp.arange(slots, dtype=jnp.int32)
    pick = slot_index[None, :] == slot_range[:, None]
    scaled = (
        gates[0].reshape(assigned, 1)
        * hidden[0].reshape(assigned, hidden_units).astype(jnp.float32)
    ).astype(jnp.bfloat16)
    lanes = -(-(hidden_units + 1) // 128) * 128
    token_tag = (jnp.arange(assigned, dtype=jnp.int32) // TOPK + 1).astype(jnp.bfloat16)
    tagged = jnp.concatenate(
        [
            scaled,
            token_tag[:, None],
            jnp.zeros((assigned, lanes - hidden_units - 1), jnp.bfloat16),
        ],
        axis=1,
    )
    hidden_slots = jnp.dot(
        pick.astype(jnp.bfloat16), tagged, preferred_element_type=jnp.float32
    ).astype(jnp.bfloat16)
    hidden_slots = hidden_slots.reshape(seq_count, EXP_DEV, CAP, lanes)
    arrived = lax.all_to_all(hidden_slots, "seq", split_axis=0, concat_axis=0, tiled=True)
    arrived_hidden = arrived[..., :hidden_units]
    slot_token = jnp.maximum(arrived[..., hidden_units].astype(jnp.int32) - 1, 0)
    wanted = jnp.arange(seq_count, dtype=jnp.int32)[:, None, None] * tokens + slot_token

    query_raw = query[0].reshape(tokens, HEADS, head_dim)
    key_raw = key_in[0].reshape(tokens, HEADS, head_dim)
    value_raw = value[0].reshape(tokens, HEADS, head_dim)
    grad_raw = cotangent[0].reshape(tokens, HEADS, head_dim)
    query_full = query_raw.astype(jnp.float32)
    key_full = key_raw.astype(jnp.float32)
    value_full = value_raw.astype(jnp.float32)
    grad_out = grad_raw.astype(jnp.float32)
    position = seq_index * tokens + jnp.arange(tokens, dtype=jnp.int32)
    scaling = 1.0 / jnp.sqrt(head_dim * (position + 1).astype(jnp.float32))
    row_scale = scaling[:, None, None]
    causal = jnp.tril(jnp.ones((tokens, tokens), jnp.float32))
    state_sum = jnp.einsum("thd,the->hde", key_raw, value_raw, preferred_element_type=jnp.float32)
    grad_sum = jnp.einsum("thd,the->hde", query_full * row_scale, grad_out, precision=PRECISE)
    scores = (
        jnp.einsum("thd,uhd->htu", query_raw, key_raw, preferred_element_type=jnp.float32) * causal
    )
    grad_scores = (
        jnp.einsum("the,uhe->htu", grad_raw, value_raw, preferred_element_type=jnp.float32) * causal
    )
    col_scale = scaling[None, :, None]
    out_local = jnp.einsum("htu,uhe->the", scores, value_full, precision=PRECISE)
    grad_q_local = jnp.einsum("htu,uhd->thd", grad_scores, key_full, precision=PRECISE)
    grad_k_local = jnp.einsum("htu,thd->uhd", grad_scores * col_scale, query_full, precision=PRECISE)
    grad_v_local = jnp.einsum("htu,the->uhe", scores * col_scale, grad_out, precision=PRECISE)
    prefix_state = jnp.zeros_like(state_sum)
    after_state = jnp.zeros_like(grad_sum)
    fwd_window = state_sum
    bwd_window = grad_sum
    shift = 1
    while shift < seq_count:
        fwd_pairs = [(src, src + shift) for src in range(seq_count - shift)]
        bwd_pairs = [(src, src - shift) for src in range(shift, seq_count)]
        fwd_arrived = lax.ppermute(fwd_window.astype(jnp.bfloat16), "seq", fwd_pairs)
        bwd_arrived = lax.ppermute(bwd_window.astype(jnp.bfloat16), "seq", bwd_pairs)
        prefix_state = prefix_state + fwd_arrived.astype(jnp.float32)
        after_state = after_state + bwd_arrived.astype(jnp.float32)
        fwd_window = state_sum + prefix_state
        bwd_window = grad_sum + after_state
        shift *= 2
    late_cotangent, prefix_state, after_state = lax.optimization_barrier(
        (cotangent, prefix_state, after_state)
    )
    halves = 2
    cols = width // halves
    scattered = []
    for half in range(halves):
        gathered = lax.all_gather(
            late_cotangent[:, :, half * cols:(half + 1) * cols], "seq", axis=1, tiled=True
        )[0]
        rows = jnp.take(gathered, wanted.reshape(-1), axis=0).reshape(
            seq_count, EXP_DEV, CAP, cols
        )
        group_term = jnp.einsum(
            "sxcf,sxcd->fxd", arrived_hidden, rows, preferred_element_type=jnp.float32
        )
        rounded = lax.optimization_barrier(group_term.astype(jnp.bfloat16))
        scattered.append(lax.psum_scatter(rounded, "grp", scatter_dimension=0, tiled=True))
    expert_grad = jnp.concatenate(scattered, axis=2).transpose(1, 0, 2)
    outputs = (
        out_local + jnp.einsum("thd,hde->the", query_full, prefix_state, precision=PRECISE)
    ) * row_scale
    grad_q = (
        grad_q_local + jnp.einsum("the,hde->thd", grad_out, prefix_state, precision=PRECISE)
    ) * row_scale
    grad_k = grad_k_local + jnp.einsum("uhe,hde->uhd", value_full, after_state, precision=PRECISE)
    grad_v = grad_v_local + jnp.einsum("uhd,hde->uhe", key_full, after_state, precision=PRECISE)

    def to_shard(array):
        return array.reshape(1, tokens, width).astype(jnp.bfloat16)

    return (to_shard(outputs), to_shard(grad_q), to_shard(grad_k), to_shard(grad_v), expert_grad)


def solution(mesh):
    in_specs = (
        P("grp", "seq", None),
        P("grp", "seq", None),
        P("grp", "seq", None),
        P("grp", "seq", None),
        P("grp", "seq", None),
        P("grp", "seq", None),
        P("grp", "seq", None, None),
    )
    out_specs = (
        P("grp", "seq", None),
        P("grp", "seq", None),
        P("grp", "seq", None),
        P("grp", "seq", None),
        P("seq", "grp", None),
    )
    return jax.shard_map(
        per_device, mesh=mesh, in_specs=in_specs, out_specs=out_specs, check_vma=False
    )
```

```python
import jax
import jax.numpy as jnp
from jax import lax
from jax.sharding import PartitionSpec as P

HEADS = 16
TOPK = 6
EXP_DEV = 2
CAP = 32


PRECISE = lax.Precision.HIGHEST


def per_device(query, key_in, value, cotangent, routes, gates, hidden):
    tokens = query.shape[1]
    width = query.shape[2]
    head_dim = width // HEADS
    hidden_units = hidden.shape[3]
    seq_count = lax.axis_size("seq")
    seq_index = lax.axis_index("seq")

    experts_total = EXP_DEV * seq_count
    assigned = tokens * TOPK
    slots = experts_total * CAP
    flat_ids = routes[0].reshape(assigned)
    expert_range = jnp.arange(experts_total, dtype=jnp.int32)
    matches = (flat_ids[:, None] == expert_range[None, :]).astype(jnp.int32)
    ranking = jnp.sum((jnp.cumsum(matches, axis=0) - matches) * matches, axis=1)
    slot_index = flat_ids * CAP + ranking
    slot_range = jnp.arange(slots, dtype=jnp.int32)
    pick = slot_index[None, :] == slot_range[:, None]
    scaled = (
        gates[0].reshape(assigned, 1)
        * hidden[0].reshape(assigned, hidden_units).astype(jnp.float32)
    ).astype(jnp.bfloat16)
    lanes = -(-(hidden_units + 1) // 128) * 128
    token_tag = (jnp.arange(assigned, dtype=jnp.int32) // TOPK + 1).astype(jnp.bfloat16)
    tagged = jnp.concatenate(
        [
            scaled,
            token_tag[:, None],
            jnp.zeros((assigned, lanes - hidden_units - 1), jnp.bfloat16),
        ],
        axis=1,
    )
    hidden_slots = jnp.dot(
        pick.astype(jnp.bfloat16), tagged, preferred_element_type=jnp.float32
    ).astype(jnp.bfloat16)
    hidden_slots = hidden_slots.reshape(seq_count, EXP_DEV, CAP, lanes)
    arrived = lax.all_to_all(hidden_slots, "seq", split_axis=0, concat_axis=0, tiled=True)
    all_cotangent = lax.all_gather(cotangent, "seq", axis=1, tiled=True)[0]
    arrived_hidden = arrived[..., :hidden_units]
    slot_token = jnp.maximum(arrived[..., hidden_units].astype(jnp.int32) - 1, 0)
    wanted = jnp.arange(seq_count, dtype=jnp.int32)[:, None, None] * tokens + slot_token

    query_raw = query[0].reshape(tokens, HEADS, head_dim)
    key_raw = key_in[0].reshape(tokens, HEADS, head_dim)
    value_raw = value[0].reshape(tokens, HEADS, head_dim)
    grad_raw = cotangent[0].reshape(tokens, HEADS, head_dim)
    query_full = query_raw.astype(jnp.float32)
    key_full = key_raw.astype(jnp.float32)
    value_full = value_raw.astype(jnp.float32)
    grad_out = grad_raw.astype(jnp.float32)
    position = seq_index * tokens + jnp.arange(tokens, dtype=jnp.int32)
    scaling = 1.0 / jnp.sqrt(head_dim * (position + 1).astype(jnp.float32))
    row_scale = scaling[:, None, None]
    causal = jnp.tril(jnp.ones((tokens, tokens), jnp.float32))
    state_sum = jnp.einsum("thd,the->hde", key_raw, value_raw, preferred_element_type=jnp.float32)
    grad_sum = jnp.einsum("thd,the->hde", query_full * row_scale, grad_out, precision=PRECISE)
    scores = (
        jnp.einsum("thd,uhd->htu", query_raw, key_raw, preferred_element_type=jnp.float32) * causal
    )
    grad_scores = (
        jnp.einsum("the,uhe->htu", grad_raw, value_raw, preferred_element_type=jnp.float32) * causal
    )
    col_scale = scaling[None, :, None]
    out_local = jnp.einsum("htu,uhe->the", scores, value_full, precision=PRECISE)
    grad_q_local = jnp.einsum("htu,uhd->thd", grad_scores, key_full, precision=PRECISE)
    grad_k_local = jnp.einsum("htu,thd->uhd", grad_scores * col_scale, query_full, precision=PRECISE)
    grad_v_local = jnp.einsum("htu,the->uhe", scores * col_scale, grad_out, precision=PRECISE)
    prefix_state = jnp.zeros_like(state_sum)
    after_state = jnp.zeros_like(grad_sum)
    fwd_window = state_sum
    bwd_window = grad_sum
    shift = 1
    while shift < seq_count:
        fwd_pairs = [(src, src + shift) for src in range(seq_count - shift)]
        bwd_pairs = [(src, src - shift) for src in range(shift, seq_count)]
        fwd_arrived = lax.ppermute(fwd_window.astype(jnp.bfloat16), "seq", fwd_pairs)
        bwd_arrived = lax.ppermute(bwd_window.astype(jnp.bfloat16), "seq", bwd_pairs)
        prefix_state = prefix_state + fwd_arrived.astype(jnp.float32)
        after_state = after_state + bwd_arrived.astype(jnp.float32)
        fwd_window = state_sum + prefix_state
        bwd_window = grad_sum + after_state
        shift *= 2
    all_cotangent, prefix_state, after_state = lax.optimization_barrier(
        (all_cotangent, prefix_state, after_state)
    )
    rows = jnp.take(all_cotangent, wanted.reshape(-1), axis=0).reshape(
        seq_count, EXP_DEV, CAP, width
    )
    group_term = jnp.einsum(
        "sxcf,sxcd->fxd", arrived_hidden, rows, preferred_element_type=jnp.float32
    )
    outputs = (
        out_local + jnp.einsum("thd,hde->the", query_full, prefix_state, precision=PRECISE)
    ) * row_scale
    grad_q = (
        grad_q_local + jnp.einsum("the,hde->thd", grad_out, prefix_state, precision=PRECISE)
    ) * row_scale
    grad_k = grad_k_local + jnp.einsum("uhe,hde->uhd", value_full, after_state, precision=PRECISE)
    grad_v = grad_v_local + jnp.einsum("uhd,hde->uhe", key_full, after_state, precision=PRECISE)

    def to_shard(array):
        return array.reshape(1, tokens, width).astype(jnp.bfloat16)

    rounded = lax.optimization_barrier(group_term.astype(jnp.bfloat16)).astype(jnp.float32)
    expert_grad = lax.psum_scatter(
        rounded.astype(jnp.bfloat16), "grp", scatter_dimension=0, tiled=True
    ).transpose(1, 0, 2)
    return (to_shard(outputs), to_shard(grad_q), to_shard(grad_k), to_shard(grad_v), expert_grad)


def solution(mesh):
    in_specs = (
        P("grp", "seq", None),
        P("grp", "seq", None),
        P("grp", "seq", None),
        P("grp", "seq", None),
        P("grp", "seq", None),
        P("grp", "seq", None),
        P("grp", "seq", None, None),
    )
    out_specs = (
        P("grp", "seq", None),
        P("grp", "seq", None),
        P("grp", "seq", None),
        P("grp", "seq", None),
        P("seq", "grp", None),
    )
    return jax.shard_map(
        per_device, mesh=mesh, in_specs=in_specs, out_specs=out_specs, check_vma=False
    )
```

```python
import jax
import jax.numpy as jnp
from jax import lax
from jax.sharding import PartitionSpec as P

HEADS = 16
TOPK = 6
EXP_DEV = 2
CAP = 32


PRECISE = lax.Precision.HIGHEST


def per_device(query, key_in, value, cotangent, routes, gates, hidden):
    tokens = query.shape[1]
    width = query.shape[2]
    head_dim = width // HEADS
    hidden_units = hidden.shape[3]
    seq_count = lax.axis_size("seq")
    seq_index = lax.axis_index("seq")

    experts_total = EXP_DEV * seq_count
    assigned = tokens * TOPK
    slots = experts_total * CAP
    flat_ids = routes[0].reshape(assigned)
    expert_range = jnp.arange(experts_total, dtype=jnp.int32)
    matches = (flat_ids[:, None] == expert_range[None, :]).astype(jnp.int32)
    ranking = jnp.sum((jnp.cumsum(matches, axis=0) - matches) * matches, axis=1)
    slot_index = flat_ids * CAP + ranking
    slot_range = jnp.arange(slots, dtype=jnp.int32)
    pick = slot_index[None, :] == slot_range[:, None]
    scaled = (
        gates[0].reshape(assigned, 1)
        * hidden[0].reshape(assigned, hidden_units).astype(jnp.float32)
    ).astype(jnp.bfloat16)
    lanes = -(-(hidden_units + 1) // 128) * 128
    token_tag = (jnp.arange(assigned, dtype=jnp.int32) // TOPK + 1).astype(jnp.bfloat16)
    tagged = jnp.concatenate(
        [
            scaled,
            token_tag[:, None],
            jnp.zeros((assigned, lanes - hidden_units - 1), jnp.bfloat16),
        ],
        axis=1,
    )
    hidden_slots = jnp.dot(
        pick.astype(jnp.bfloat16), tagged, preferred_element_type=jnp.float32
    ).astype(jnp.bfloat16)
    hidden_slots = hidden_slots.reshape(seq_count, EXP_DEV, CAP, lanes)
    arrived = lax.all_to_all(hidden_slots, "seq", split_axis=0, concat_axis=0, tiled=True)
    all_cotangent = lax.all_gather(cotangent, "seq", axis=1, tiled=True)[0]
    arrived_hidden = arrived[..., :hidden_units]
    slot_token = arrived[..., hidden_units].astype(jnp.int32) - 1
    token_pick = (
        slot_token[:, :, None, :] == jnp.arange(tokens, dtype=jnp.int32)[None, None, :, None]
    ).astype(jnp.bfloat16)
    token_weights = jnp.einsum(
        "sxtc,sxcf->fxst", token_pick, arrived_hidden, preferred_element_type=jnp.float32
    ).astype(jnp.bfloat16).reshape(hidden_units * EXP_DEV, seq_count * tokens)

    query_raw = query[0].reshape(tokens, HEADS, head_dim)
    key_raw = key_in[0].reshape(tokens, HEADS, head_dim)
    value_raw = value[0].reshape(tokens, HEADS, head_dim)
    grad_raw = cotangent[0].reshape(tokens, HEADS, head_dim)
    query_full = query_raw.astype(jnp.float32)
    key_full = key_raw.astype(jnp.float32)
    value_full = value_raw.astype(jnp.float32)
    grad_out = grad_raw.astype(jnp.float32)
    position = seq_index * tokens + jnp.arange(tokens, dtype=jnp.int32)
    scaling = 1.0 / jnp.sqrt(head_dim * (position + 1).astype(jnp.float32))
    row_scale = scaling[:, None, None]
    causal = jnp.tril(jnp.ones((tokens, tokens), jnp.float32))
    state_sum = jnp.einsum("thd,the->hde", key_raw, value_raw, preferred_element_type=jnp.float32)
    grad_sum = jnp.einsum("thd,the->hde", query_full * row_scale, grad_out, precision=PRECISE)
    scores = (
        jnp.einsum("thd,uhd->htu", query_raw, key_raw, preferred_element_type=jnp.float32) * causal
    )
    grad_scores = (
        jnp.einsum("the,uhe->htu", grad_raw, value_raw, preferred_element_type=jnp.float32) * causal
    )
    col_scale = scaling[None, :, None]
    out_local = jnp.einsum("htu,uhe->the", scores, value_full, precision=PRECISE)
    grad_q_local = jnp.einsum("htu,uhd->thd", grad_scores, key_full, precision=PRECISE)
    grad_k_local = jnp.einsum("htu,thd->uhd", grad_scores * col_scale, query_full, precision=PRECISE)
    grad_v_local = jnp.einsum("htu,the->uhe", scores * col_scale, grad_out, precision=PRECISE)
    prefix_state = jnp.zeros_like(state_sum)
    after_state = jnp.zeros_like(grad_sum)
    fwd_window = state_sum
    bwd_window = grad_sum
    shift = 1
    while shift < seq_count:
        fwd_pairs = [(src, src + shift) for src in range(seq_count - shift)]
        bwd_pairs = [(src, src - shift) for src in range(shift, seq_count)]
        fwd_arrived = lax.ppermute(fwd_window.astype(jnp.bfloat16), "seq", fwd_pairs)
        bwd_arrived = lax.ppermute(bwd_window.astype(jnp.bfloat16), "seq", bwd_pairs)
        prefix_state = prefix_state + fwd_arrived.astype(jnp.float32)
        after_state = after_state + bwd_arrived.astype(jnp.float32)
        fwd_window = state_sum + prefix_state
        bwd_window = grad_sum + after_state
        shift *= 2
    all_cotangent, prefix_state, after_state = lax.optimization_barrier(
        (all_cotangent, prefix_state, after_state)
    )
    group_term = jnp.dot(
        token_weights, all_cotangent, preferred_element_type=jnp.float32
    ).reshape(hidden_units, EXP_DEV, width)
    outputs = (
        out_local + jnp.einsum("thd,hde->the", query_full, prefix_state, precision=PRECISE)
    ) * row_scale
    grad_q = (
        grad_q_local + jnp.einsum("the,hde->thd", grad_out, prefix_state, precision=PRECISE)
    ) * row_scale
    grad_k = grad_k_local + jnp.einsum("uhe,hde->uhd", value_full, after_state, precision=PRECISE)
    grad_v = grad_v_local + jnp.einsum("uhd,hde->uhe", key_full, after_state, precision=PRECISE)

    def to_shard(array):
        return array.reshape(1, tokens, width).astype(jnp.bfloat16)

    rounded = lax.optimization_barrier(group_term.astype(jnp.bfloat16)).astype(jnp.float32)
    expert_grad = lax.psum_scatter(
        rounded.astype(jnp.bfloat16), "grp", scatter_dimension=0, tiled=True
    ).transpose(1, 0, 2)
    return (to_shard(outputs), to_shard(grad_q), to_shard(grad_k), to_shard(grad_v), expert_grad)


def solution(mesh):
    in_specs = (
        P("grp", "seq", None),
        P("grp", "seq", None),
        P("grp", "seq", None),
        P("grp", "seq", None),
        P("grp", "seq", None),
        P("grp", "seq", None),
        P("grp", "seq", None, None),
    )
    out_specs = (
        P("grp", "seq", None),
        P("grp", "seq", None),
        P("grp", "seq", None),
        P("grp", "seq", None),
        P("seq", "grp", None),
    )
    return jax.shard_map(
        per_device, mesh=mesh, in_specs=in_specs, out_specs=out_specs, check_vma=False
    )
```

```python
import jax
import jax.numpy as jnp
from jax import lax
from jax.sharding import PartitionSpec as P

HEADS = 16
TOPK = 6
EXP_DEV = 2
CAP = 32


PRECISE = lax.Precision.HIGHEST


def per_device(query, key_in, value, cotangent, routes, gates, hidden):
    tokens = query.shape[1]
    width = query.shape[2]
    head_dim = width // HEADS
    hidden_units = hidden.shape[3]
    seq_count = lax.axis_size("seq")
    seq_index = lax.axis_index("seq")

    experts_total = EXP_DEV * seq_count
    assigned = tokens * TOPK
    slots = experts_total * CAP
    flat_ids = routes[0].reshape(assigned)
    expert_range = jnp.arange(experts_total, dtype=jnp.int32)
    matches = (flat_ids[:, None] == expert_range[None, :]).astype(jnp.int32)
    ranking = jnp.sum((jnp.cumsum(matches, axis=0) - matches) * matches, axis=1)
    slot_index = flat_ids * CAP + ranking
    slot_range = jnp.arange(slots, dtype=jnp.int32)
    pick = slot_index[None, :] == slot_range[:, None]
    scaled = (
        gates[0].reshape(assigned, 1)
        * hidden[0].reshape(assigned, hidden_units).astype(jnp.float32)
    ).astype(jnp.bfloat16)
    lanes = -(-(hidden_units + 1) // 128) * 128
    token_tag = (jnp.arange(assigned, dtype=jnp.int32) // TOPK + 1).astype(jnp.bfloat16)
    tagged = jnp.concatenate(
        [
            scaled,
            token_tag[:, None],
            jnp.zeros((assigned, lanes - hidden_units - 1), jnp.bfloat16),
        ],
        axis=1,
    )
    hidden_slots = jnp.dot(
        pick.astype(jnp.bfloat16), tagged, preferred_element_type=jnp.float32
    ).astype(jnp.bfloat16)
    hidden_slots = hidden_slots.reshape(seq_count, EXP_DEV, CAP, lanes)
    arrived = lax.all_to_all(hidden_slots, "seq", split_axis=0, concat_axis=0, tiled=True)
    all_cotangent = lax.all_gather(cotangent, "seq", axis=1, tiled=True)[0]
    arrived_hidden = arrived[..., :hidden_units]
    slot_token = arrived[..., hidden_units].astype(jnp.int32) - 1
    token_pick = (
        slot_token[:, :, None, :] == jnp.arange(tokens, dtype=jnp.int32)[None, None, :, None]
    ).astype(jnp.bfloat16)
    token_weights = jnp.einsum(
        "sxtc,sxcf->fxst", token_pick, arrived_hidden, preferred_element_type=jnp.float32
    ).astype(jnp.bfloat16).reshape(hidden_units * EXP_DEV, seq_count * tokens)

    query_raw = query[0].reshape(tokens, HEADS, head_dim)
    key_raw = key_in[0].reshape(tokens, HEADS, head_dim)
    value_raw = value[0].reshape(tokens, HEADS, head_dim)
    grad_raw = cotangent[0].reshape(tokens, HEADS, head_dim)
    query_full = query_raw.astype(jnp.float32)
    key_full = key_raw.astype(jnp.float32)
    value_full = value_raw.astype(jnp.float32)
    grad_out = grad_raw.astype(jnp.float32)
    position = seq_index * tokens + jnp.arange(tokens, dtype=jnp.int32)
    scaling = 1.0 / jnp.sqrt(head_dim * (position + 1).astype(jnp.float32))
    row_scale = scaling[:, None, None]
    causal = jnp.tril(jnp.ones((tokens, tokens), jnp.float32))
    state_sum = jnp.einsum("thd,the->hde", key_raw, value_raw, preferred_element_type=jnp.float32)
    grad_sum = jnp.einsum("thd,the->hde", query_full * row_scale, grad_out, precision=PRECISE)
    scores = (
        jnp.einsum("thd,uhd->htu", query_raw, key_raw, preferred_element_type=jnp.float32) * causal
    )
    grad_scores = (
        jnp.einsum("the,uhe->htu", grad_raw, value_raw, preferred_element_type=jnp.float32) * causal
    )
    col_scale = scaling[None, :, None]
    out_local = jnp.einsum("htu,uhe->the", scores, value_full, precision=PRECISE)
    grad_q_local = jnp.einsum("htu,uhd->thd", grad_scores, key_full, precision=PRECISE)
    grad_k_local = jnp.einsum("htu,thd->uhd", grad_scores * col_scale, query_full, precision=PRECISE)
    grad_v_local = jnp.einsum("htu,the->uhe", scores * col_scale, grad_out, precision=PRECISE)
    prefix_state = jnp.zeros_like(state_sum)
    after_state = jnp.zeros_like(grad_sum)
    fwd_window = state_sum
    bwd_window = grad_sum
    shift = 1
    while shift < seq_count:
        fwd_pairs = [(src, src + shift) for src in range(seq_count - shift)]
        bwd_pairs = [(src, src - shift) for src in range(shift, seq_count)]
        fwd_sent = fwd_window.astype(jnp.bfloat16)
        bwd_sent = bwd_window.astype(jnp.bfloat16)
        if shift == 8:
            token_weights, fwd_sent, bwd_sent = lax.optimization_barrier(
                (token_weights, fwd_sent, bwd_sent)
            )
        fwd_arrived = lax.ppermute(fwd_sent, "seq", fwd_pairs)
        bwd_arrived = lax.ppermute(bwd_sent, "seq", bwd_pairs)
        prefix_state = prefix_state + fwd_arrived.astype(jnp.float32)
        after_state = after_state + bwd_arrived.astype(jnp.float32)
        fwd_window = state_sum + prefix_state
        bwd_window = grad_sum + after_state
        shift *= 2
    all_cotangent, prefix_state, after_state = lax.optimization_barrier(
        (all_cotangent, prefix_state, after_state)
    )
    group_term = jnp.dot(
        token_weights, all_cotangent, preferred_element_type=jnp.float32
    ).reshape(hidden_units, EXP_DEV, width)
    outputs = (
        out_local + jnp.einsum("thd,hde->the", query_full, prefix_state, precision=PRECISE)
    ) * row_scale
    grad_q = (
        grad_q_local + jnp.einsum("the,hde->thd", grad_out, prefix_state, precision=PRECISE)
    ) * row_scale
    grad_k = grad_k_local + jnp.einsum("uhe,hde->uhd", value_full, after_state, precision=PRECISE)
    grad_v = grad_v_local + jnp.einsum("uhd,hde->uhe", key_full, after_state, precision=PRECISE)

    def to_shard(array):
        return array.reshape(1, tokens, width).astype(jnp.bfloat16)

    rounded = lax.optimization_barrier(group_term.astype(jnp.bfloat16)).astype(jnp.float32)
    expert_grad = lax.psum_scatter(
        rounded.astype(jnp.bfloat16), "grp", scatter_dimension=0, tiled=True
    ).transpose(1, 0, 2)
    return (to_shard(outputs), to_shard(grad_q), to_shard(grad_k), to_shard(grad_v), expert_grad)


def solution(mesh):
    in_specs = (
        P("grp", "seq", None),
        P("grp", "seq", None),
        P("grp", "seq", None),
        P("grp", "seq", None),
        P("grp", "seq", None),
        P("grp", "seq", None),
        P("grp", "seq", None, None),
    )
    out_specs = (
        P("grp", "seq", None),
        P("grp", "seq", None),
        P("grp", "seq", None),
        P("grp", "seq", None),
        P("seq", "grp", None),
    )
    return jax.shard_map(
        per_device, mesh=mesh, in_specs=in_specs, out_specs=out_specs, check_vma=False
    )
```

```python
import jax
import jax.numpy as jnp
from jax import lax
from jax.sharding import PartitionSpec as P

HEADS = 16
TOPK = 6
EXP_DEV = 2
CAP = 32


PRECISE = lax.Precision.HIGHEST


def per_device(query, key_in, value, cotangent, routes, gates, hidden):
    tokens = query.shape[1]
    width = query.shape[2]
    head_dim = width // HEADS
    hidden_units = hidden.shape[3]
    seq_count = lax.axis_size("seq")
    seq_index = lax.axis_index("seq")

    experts_total = EXP_DEV * seq_count
    assigned = tokens * TOPK
    slots = experts_total * CAP
    flat_ids = routes[0].reshape(assigned)
    expert_range = jnp.arange(experts_total, dtype=jnp.int32)
    matches = (flat_ids[:, None] == expert_range[None, :]).astype(jnp.int32)
    ranking = jnp.sum((jnp.cumsum(matches, axis=0) - matches) * matches, axis=1)
    slot_index = flat_ids * CAP + ranking
    slot_range = jnp.arange(slots, dtype=jnp.int32)
    pick = slot_index[None, :] == slot_range[:, None]
    scaled = (
        gates[0].reshape(assigned, 1)
        * hidden[0].reshape(assigned, hidden_units).astype(jnp.float32)
    ).astype(jnp.bfloat16)
    lanes = -(-(hidden_units + 1) // 128) * 128
    token_tag = (jnp.arange(assigned, dtype=jnp.int32) // TOPK + 1).astype(jnp.bfloat16)
    tagged = jnp.concatenate(
        [
            scaled,
            token_tag[:, None],
            jnp.zeros((assigned, lanes - hidden_units - 1), jnp.bfloat16),
        ],
        axis=1,
    )
    hidden_slots = jnp.dot(
        pick.astype(jnp.bfloat16), tagged, preferred_element_type=jnp.float32
    ).astype(jnp.bfloat16)
    hidden_slots = hidden_slots.reshape(seq_count, EXP_DEV, CAP, lanes)
    arrived = lax.all_to_all(hidden_slots, "seq", split_axis=0, concat_axis=0, tiled=True)
    all_cotangent = lax.all_gather(cotangent, "seq", axis=1, tiled=True)[0]
    arrived_hidden = arrived[..., :hidden_units]
    slot_token = arrived[..., hidden_units].astype(jnp.int32) - 1
    token_pick = (
        slot_token[:, :, None, :] == jnp.arange(tokens, dtype=jnp.int32)[None, None, :, None]
    ).astype(jnp.bfloat16)
    token_weights = jnp.einsum(
        "sxtc,sxcf->fxst", token_pick, arrived_hidden, preferred_element_type=jnp.float32
    ).astype(jnp.bfloat16).reshape(hidden_units * EXP_DEV, seq_count * tokens)

    query_raw = query[0].reshape(tokens, HEADS, head_dim)
    key_raw = key_in[0].reshape(tokens, HEADS, head_dim)
    value_raw = value[0].reshape(tokens, HEADS, head_dim)
    grad_raw = cotangent[0].reshape(tokens, HEADS, head_dim)
    query_full = query_raw.astype(jnp.float32)
    key_full = key_raw.astype(jnp.float32)
    value_full = value_raw.astype(jnp.float32)
    grad_out = grad_raw.astype(jnp.float32)
    position = seq_index * tokens + jnp.arange(tokens, dtype=jnp.int32)
    scaling = 1.0 / jnp.sqrt(head_dim * (position + 1).astype(jnp.float32))
    row_scale = scaling[:, None, None]
    causal = jnp.tril(jnp.ones((tokens, tokens), jnp.float32))
    state_sum = jnp.einsum("thd,the->hde", key_raw, value_raw, preferred_element_type=jnp.float32)
    grad_sum = jnp.einsum("thd,the->hde", query_full * row_scale, grad_out, precision=PRECISE)
    scores = (
        jnp.einsum("thd,uhd->htu", query_raw, key_raw, preferred_element_type=jnp.float32) * causal
    )
    grad_scores = (
        jnp.einsum("the,uhe->htu", grad_raw, value_raw, preferred_element_type=jnp.float32) * causal
    )
    col_scale = scaling[None, :, None]
    out_local = jnp.einsum("htu,uhe->the", scores, value_full, precision=PRECISE)
    grad_q_local = jnp.einsum("htu,uhd->thd", grad_scores, key_full, precision=PRECISE)
    grad_k_local = jnp.einsum("htu,thd->uhd", grad_scores * col_scale, query_full, precision=PRECISE)
    grad_v_local = jnp.einsum("htu,the->uhe", scores * col_scale, grad_out, precision=PRECISE)
    prefix_state = jnp.zeros_like(state_sum)
    after_state = jnp.zeros_like(grad_sum)
    fwd_window = state_sum
    bwd_window = grad_sum
    shift = 1
    while shift < seq_count:
        fwd_pairs = [(src, src + shift) for src in range(seq_count - shift)]
        bwd_pairs = [(src, src - shift) for src in range(shift, seq_count)]
        fwd_arrived = lax.ppermute(fwd_window.astype(jnp.bfloat16), "seq", fwd_pairs)
        bwd_arrived = lax.ppermute(bwd_window.astype(jnp.bfloat16), "seq", bwd_pairs)
        if 2 * shift == seq_count // 2:
            all_cotangent, fwd_arrived, bwd_arrived = lax.optimization_barrier(
                (all_cotangent, fwd_arrived, bwd_arrived)
            )
        prefix_state = prefix_state + fwd_arrived.astype(jnp.float32)
        after_state = after_state + bwd_arrived.astype(jnp.float32)
        fwd_window = state_sum + prefix_state
        bwd_window = grad_sum + after_state
        shift *= 2
    group_term = jnp.dot(
        token_weights, all_cotangent, preferred_element_type=jnp.float32
    ).reshape(hidden_units, EXP_DEV, width)
    outputs = (
        out_local + jnp.einsum("thd,hde->the", query_full, prefix_state, precision=PRECISE)
    ) * row_scale
    grad_q = (
        grad_q_local + jnp.einsum("the,hde->thd", grad_out, prefix_state, precision=PRECISE)
    ) * row_scale
    grad_k = grad_k_local + jnp.einsum("uhe,hde->uhd", value_full, after_state, precision=PRECISE)
    grad_v = grad_v_local + jnp.einsum("uhd,hde->uhe", key_full, after_state, precision=PRECISE)

    def to_shard(array):
        return array.reshape(1, tokens, width).astype(jnp.bfloat16)

    rounded = lax.optimization_barrier(group_term.astype(jnp.bfloat16)).astype(jnp.float32)
    expert_grad = lax.psum_scatter(
        rounded.astype(jnp.bfloat16), "grp", scatter_dimension=0, tiled=True
    ).transpose(1, 0, 2)
    return (to_shard(outputs), to_shard(grad_q), to_shard(grad_k), to_shard(grad_v), expert_grad)


def solution(mesh):
    in_specs = (
        P("grp", "seq", None),
        P("grp", "seq", None),
        P("grp", "seq", None),
        P("grp", "seq", None),
        P("grp", "seq", None),
        P("grp", "seq", None),
        P("grp", "seq", None, None),
    )
    out_specs = (
        P("grp", "seq", None),
        P("grp", "seq", None),
        P("grp", "seq", None),
        P("grp", "seq", None),
        P("seq", "grp", None),
    )
    return jax.shard_map(
        per_device, mesh=mesh, in_specs=in_specs, out_specs=out_specs, check_vma=False
    )
```

```python
import jax
import jax.numpy as jnp
from jax import lax
from jax.sharding import PartitionSpec as P

HEADS = 16
TOPK = 6
EXP_DEV = 2
CAP = 32


PRECISE = lax.Precision.HIGHEST


def per_device(query, key_in, value, cotangent, routes, gates, hidden):
    tokens = query.shape[1]
    width = query.shape[2]
    head_dim = width // HEADS
    hidden_units = hidden.shape[3]
    seq_count = lax.axis_size("seq")
    seq_index = lax.axis_index("seq")

    experts_total = EXP_DEV * seq_count
    assigned = tokens * TOPK
    slots = experts_total * CAP
    flat_ids = routes[0].reshape(assigned)
    expert_range = jnp.arange(experts_total, dtype=jnp.int32)
    matches = (flat_ids[:, None] == expert_range[None, :]).astype(jnp.int32)
    ranking = jnp.sum((jnp.cumsum(matches, axis=0) - matches) * matches, axis=1)
    slot_index = flat_ids * CAP + ranking
    slot_range = jnp.arange(slots, dtype=jnp.int32)
    pick = slot_index[None, :] == slot_range[:, None]
    scaled = (
        gates[0].reshape(assigned, 1)
        * hidden[0].reshape(assigned, hidden_units).astype(jnp.float32)
    ).astype(jnp.bfloat16)
    lanes = -(-(hidden_units + 1) // 128) * 128
    token_tag = (jnp.arange(assigned, dtype=jnp.int32) // TOPK + 1).astype(jnp.bfloat16)
    tagged = jnp.concatenate(
        [
            scaled,
            token_tag[:, None],
            jnp.zeros((assigned, lanes - hidden_units - 1), jnp.bfloat16),
        ],
        axis=1,
    )
    hidden_slots = jnp.dot(
        pick.astype(jnp.bfloat16), tagged, preferred_element_type=jnp.float32
    ).astype(jnp.bfloat16)
    hidden_slots = hidden_slots.reshape(seq_count, EXP_DEV, CAP, lanes)
    arrived = lax.all_to_all(hidden_slots, "seq", split_axis=0, concat_axis=0, tiled=True)
    all_cotangent = lax.all_gather(cotangent, "seq", axis=1, tiled=True)[0]
    arrived_hidden = arrived[..., :hidden_units]
    slot_token = arrived[..., hidden_units].astype(jnp.int32) - 1
    token_pick = (
        slot_token[:, :, None, :] == jnp.arange(tokens, dtype=jnp.int32)[None, None, :, None]
    ).astype(jnp.bfloat16)
    token_weights = jnp.einsum(
        "sxtc,sxcf->fxst", token_pick, arrived_hidden, preferred_element_type=jnp.float32
    ).astype(jnp.bfloat16).reshape(hidden_units * EXP_DEV, seq_count * tokens)

    query_raw = query[0].reshape(tokens, HEADS, head_dim)
    key_raw = key_in[0].reshape(tokens, HEADS, head_dim)
    value_raw = value[0].reshape(tokens, HEADS, head_dim)
    grad_raw = cotangent[0].reshape(tokens, HEADS, head_dim)
    query_full = query_raw.astype(jnp.float32)
    key_full = key_raw.astype(jnp.float32)
    value_full = value_raw.astype(jnp.float32)
    grad_out = grad_raw.astype(jnp.float32)
    position = seq_index * tokens + jnp.arange(tokens, dtype=jnp.int32)
    scaling = 1.0 / jnp.sqrt(head_dim * (position + 1).astype(jnp.float32))
    row_scale = scaling[:, None, None]
    causal = jnp.tril(jnp.ones((tokens, tokens), jnp.float32))
    state_sum = jnp.einsum("thd,the->hde", key_raw, value_raw, preferred_element_type=jnp.float32)
    grad_sum = jnp.einsum("thd,the->hde", query_full * row_scale, grad_out, precision=PRECISE)
    scores = (
        jnp.einsum("thd,uhd->htu", query_raw, key_raw, preferred_element_type=jnp.float32) * causal
    )
    grad_scores = (
        jnp.einsum("the,uhe->htu", grad_raw, value_raw, preferred_element_type=jnp.float32) * causal
    )
    col_scale = scaling[None, :, None]
    out_local = jnp.einsum("htu,uhe->the", scores, value_full, precision=PRECISE)
    grad_q_local = jnp.einsum("htu,uhd->thd", grad_scores, key_full, precision=PRECISE)
    grad_k_local = jnp.einsum("htu,thd->uhd", grad_scores * col_scale, query_full, precision=PRECISE)
    grad_v_local = jnp.einsum("htu,the->uhe", scores * col_scale, grad_out, precision=PRECISE)
    prefix_state = jnp.zeros_like(state_sum)
    after_state = jnp.zeros_like(grad_sum)
    fwd_window = state_sum
    bwd_window = grad_sum
    shifts = []
    shift = 1
    while shift < seq_count:
        shifts.append(shift)
        shift *= 2
    if len(shifts) >= 3:
        shifts = shifts[:2] + shifts[3:] + [shifts[2]]
    for step, shift in enumerate(shifts):
        fwd_pairs = [(src, src + shift) for src in range(seq_count - shift)]
        bwd_pairs = [(src, src - shift) for src in range(shift, seq_count)]
        fwd_arrived = lax.ppermute(fwd_window.astype(jnp.bfloat16), "seq", fwd_pairs)
        bwd_arrived = lax.ppermute(bwd_window.astype(jnp.bfloat16), "seq", bwd_pairs)
        if step == len(shifts) - 2:
            all_cotangent, fwd_arrived, bwd_arrived = lax.optimization_barrier(
                (all_cotangent, fwd_arrived, bwd_arrived)
            )
        prefix_state = prefix_state + fwd_arrived.astype(jnp.float32)
        after_state = after_state + bwd_arrived.astype(jnp.float32)
        fwd_window = state_sum + prefix_state
        bwd_window = grad_sum + after_state
    group_term = jnp.dot(
        token_weights, all_cotangent, preferred_element_type=jnp.float32
    ).reshape(hidden_units, EXP_DEV, width)
    outputs = (
        out_local + jnp.einsum("thd,hde->the", query_full, prefix_state, precision=PRECISE)
    ) * row_scale
    grad_q = (
        grad_q_local + jnp.einsum("the,hde->thd", grad_out, prefix_state, precision=PRECISE)
    ) * row_scale
    grad_k = grad_k_local + jnp.einsum("uhe,hde->uhd", value_full, after_state, precision=PRECISE)
    grad_v = grad_v_local + jnp.einsum("uhd,hde->uhe", key_full, after_state, precision=PRECISE)

    def to_shard(array):
        return array.reshape(1, tokens, width).astype(jnp.bfloat16)

    rounded = lax.optimization_barrier(group_term.astype(jnp.bfloat16)).astype(jnp.float32)
    expert_grad = lax.psum_scatter(
        rounded.astype(jnp.bfloat16), "grp", scatter_dimension=0, tiled=True
    ).transpose(1, 0, 2)
    return (to_shard(outputs), to_shard(grad_q), to_shard(grad_k), to_shard(grad_v), expert_grad)


def solution(mesh):
    in_specs = (
        P("grp", "seq", None),
        P("grp", "seq", None),
        P("grp", "seq", None),
        P("grp", "seq", None),
        P("grp", "seq", None),
        P("grp", "seq", None),
        P("grp", "seq", None, None),
    )
    out_specs = (
        P("grp", "seq", None),
        P("grp", "seq", None),
        P("grp", "seq", None),
        P("grp", "seq", None),
        P("seq", "grp", None),
    )
    return jax.shard_map(
        per_device, mesh=mesh, in_specs=in_specs, out_specs=out_specs, check_vma=False
    )
```

```python
import jax
import jax.numpy as jnp
from jax import lax
from jax.sharding import PartitionSpec as P

HEADS = 16
TOPK = 6
EXP_DEV = 2
CAP = 32


PRECISE = lax.Precision.HIGHEST


def per_device(query, key_in, value, cotangent, routes, gates, hidden):
    tokens = query.shape[1]
    width = query.shape[2]
    head_dim = width // HEADS
    hidden_units = hidden.shape[3]
    seq_count = lax.axis_size("seq")
    seq_index = lax.axis_index("seq")

    experts_total = EXP_DEV * seq_count
    assigned = tokens * TOPK
    slots = experts_total * CAP
    flat_ids = routes[0].reshape(assigned)
    expert_range = jnp.arange(experts_total, dtype=jnp.int32)
    matches = (flat_ids[:, None] == expert_range[None, :]).astype(jnp.int32)
    ranking = jnp.sum((jnp.cumsum(matches, axis=0) - matches) * matches, axis=1)
    slot_index = flat_ids * CAP + ranking
    slot_range = jnp.arange(slots, dtype=jnp.int32)
    pick = slot_index[None, :] == slot_range[:, None]
    scaled = (
        gates[0].reshape(assigned, 1)
        * hidden[0].reshape(assigned, hidden_units).astype(jnp.float32)
    ).astype(jnp.bfloat16)
    lanes = -(-(hidden_units + 1) // 128) * 128
    token_tag = (jnp.arange(assigned, dtype=jnp.int32) // TOPK + 1).astype(jnp.bfloat16)
    tagged = jnp.concatenate(
        [
            scaled,
            token_tag[:, None],
            jnp.zeros((assigned, lanes - hidden_units - 1), jnp.bfloat16),
        ],
        axis=1,
    )
    hidden_slots = jnp.dot(
        pick.astype(jnp.bfloat16), tagged, preferred_element_type=jnp.float32
    ).astype(jnp.bfloat16)
    hidden_slots = hidden_slots.reshape(seq_count, EXP_DEV, CAP, lanes)
    arrived = lax.all_to_all(hidden_slots, "seq", split_axis=0, concat_axis=0, tiled=True)
    all_cotangent = lax.all_gather(cotangent, "seq", axis=1, tiled=True)[0]
    arrived_hidden = arrived[..., :hidden_units]
    slot_token = arrived[..., hidden_units].astype(jnp.int32) - 1
    token_pick = (
        slot_token[:, :, None, :] == jnp.arange(tokens, dtype=jnp.int32)[None, None, :, None]
    ).astype(jnp.bfloat16)
    token_weights = jnp.einsum(
        "sxtc,sxcf->fxst", token_pick, arrived_hidden, preferred_element_type=jnp.float32
    ).astype(jnp.bfloat16).reshape(hidden_units * EXP_DEV, seq_count * tokens)

    query_raw = query[0].reshape(tokens, HEADS, head_dim)
    key_raw = key_in[0].reshape(tokens, HEADS, head_dim)
    value_raw = value[0].reshape(tokens, HEADS, head_dim)
    grad_raw = cotangent[0].reshape(tokens, HEADS, head_dim)
    query_full = query_raw.astype(jnp.float32)
    key_full = key_raw.astype(jnp.float32)
    value_full = value_raw.astype(jnp.float32)
    grad_out = grad_raw.astype(jnp.float32)
    position = seq_index * tokens + jnp.arange(tokens, dtype=jnp.int32)
    scaling = 1.0 / jnp.sqrt(head_dim * (position + 1).astype(jnp.float32))
    row_scale = scaling[:, None, None]
    causal = jnp.tril(jnp.ones((tokens, tokens), jnp.float32))
    state_sum = jnp.einsum("thd,the->hde", key_raw, value_raw, preferred_element_type=jnp.float32)
    grad_sum = jnp.einsum("thd,the->hde", query_full * row_scale, grad_out, precision=PRECISE)
    scores = (
        jnp.einsum("thd,uhd->htu", query_raw, key_raw, preferred_element_type=jnp.float32) * causal
    )
    grad_scores = (
        jnp.einsum("the,uhe->htu", grad_raw, value_raw, preferred_element_type=jnp.float32) * causal
    )
    col_scale = scaling[None, :, None]
    out_local = jnp.einsum("htu,uhe->the", scores, value_full, precision=PRECISE)
    grad_q_local = jnp.einsum("htu,uhd->thd", grad_scores, key_full, precision=PRECISE)
    grad_k_local = jnp.einsum("htu,thd->uhd", grad_scores * col_scale, query_full, precision=PRECISE)
    grad_v_local = jnp.einsum("htu,the->uhe", scores * col_scale, grad_out, precision=PRECISE)
    prefix_state = jnp.zeros_like(state_sum)
    after_state = jnp.zeros_like(grad_sum)
    fwd_window = state_sum
    bwd_window = grad_sum
    shifts = []
    shift = 1
    while shift < seq_count:
        shifts.append(shift)
        shift *= 2
    if len(shifts) >= 3:
        shifts = shifts[:1] + shifts[3:] + shifts[1:3]
    for step, shift in enumerate(shifts):
        fwd_pairs = [(src, src + shift) for src in range(seq_count - shift)]
        bwd_pairs = [(src, src - shift) for src in range(shift, seq_count)]
        fwd_arrived = lax.ppermute(fwd_window.astype(jnp.bfloat16), "seq", fwd_pairs)
        bwd_arrived = lax.ppermute(bwd_window.astype(jnp.bfloat16), "seq", bwd_pairs)
        if step == len(shifts) - 3:
            all_cotangent, fwd_arrived, bwd_arrived = lax.optimization_barrier(
                (all_cotangent, fwd_arrived, bwd_arrived)
            )
        prefix_state = prefix_state + fwd_arrived.astype(jnp.float32)
        after_state = after_state + bwd_arrived.astype(jnp.float32)
        fwd_window = state_sum + prefix_state
        bwd_window = grad_sum + after_state
    group_term = jnp.dot(
        token_weights, all_cotangent, preferred_element_type=jnp.float32
    ).reshape(hidden_units, EXP_DEV, width)
    outputs = (
        out_local + jnp.einsum("thd,hde->the", query_full, prefix_state, precision=PRECISE)
    ) * row_scale
    grad_q = (
        grad_q_local + jnp.einsum("the,hde->thd", grad_out, prefix_state, precision=PRECISE)
    ) * row_scale
    grad_k = grad_k_local + jnp.einsum("uhe,hde->uhd", value_full, after_state, precision=PRECISE)
    grad_v = grad_v_local + jnp.einsum("uhd,hde->uhe", key_full, after_state, precision=PRECISE)

    def to_shard(array):
        return array.reshape(1, tokens, width).astype(jnp.bfloat16)

    rounded = lax.optimization_barrier(group_term.astype(jnp.bfloat16)).astype(jnp.float32)
    expert_grad = lax.psum_scatter(
        rounded.astype(jnp.bfloat16), "grp", scatter_dimension=0, tiled=True
    ).transpose(1, 0, 2)
    return (to_shard(outputs), to_shard(grad_q), to_shard(grad_k), to_shard(grad_v), expert_grad)


def solution(mesh):
    in_specs = (
        P("grp", "seq", None),
        P("grp", "seq", None),
        P("grp", "seq", None),
        P("grp", "seq", None),
        P("grp", "seq", None),
        P("grp", "seq", None),
        P("grp", "seq", None, None),
    )
    out_specs = (
        P("grp", "seq", None),
        P("grp", "seq", None),
        P("grp", "seq", None),
        P("grp", "seq", None),
        P("seq", "grp", None),
    )
    return jax.shard_map(
        per_device, mesh=mesh, in_specs=in_specs, out_specs=out_specs, check_vma=False
    )
```
